768 devices in a mesh: chan: 32 (over z_lo, y), row: 8 (over x, core), col: 3 (over z_hi).
Axes of the slice: x: 4, y: 8, z: 12 (z_hi: 3, z_lo: 4; z = z_hi * 4 + z_lo), core: 2. Of those that a mesh axis runs over, the one named last changes fastest.
Arguments:
- voltages: bfloat16 [24, 64, 2, 16, 128], P(('row', 'col'), 'chan'), may hold values from -270 to 270
- source_flux: float32 [128, 64], P('chan'), may hold values from 0.1 to 10
- initial_gains: float32 [128, 2, 24, 64], P('chan', None, ('row', 'col')), may hold values from -4 to 4
- antenna_positions: float32 [2, 24, 64], replicated, may hold values from -1 to 1
- flagged: int32 [24, 64], replicated, may hold values 0 or 1
- source_pixels: int32 [64, 2], replicated, may hold values from 0 to 255
Outputs:
- gains: float32 [128, 2, 24, 64], P('chan', None, ('row', 'col'))
The draws below stay inside these ranges and needn't reach their ends.
Inputs may be any that keep to these rules, and one draw needn't show every extreme that they name: flagged holds 0 or 1 for each antenna, the same for all channels.
All inputs are finite; a program needn't handle non-finite values.
Results may differ from the reference program's by a relative error of at most 0.012.
Values may be sent and summed in bfloat16 or wider, within the bound.
No kernel may reach another device: no remote copies, remote signals or barrier semaphores. Data moves between devices by JAX's collectives and lax.ppermute only.
A program may use at most 32 MiB of HBM per device.

```python
import math
import jax
import jax.numpy as jnp
from jax import lax

SNAP = 16
SOURCES = 64
PIX = 256
ITERS = 3
CHANS = 128
GROUPS = 24
SUBANT = 64


def touch_ends(drawn, key, low, top_value):
    spot = [jax.random.randint(jax.random.fold_in(key, axis), (), 0, length) for axis, length in enumerate(drawn.shape)]
    main_axis = drawn.shape.index(max(drawn.shape))
    next_to = spot[:main_axis] + [(spot[main_axis] + 1) % drawn.shape[main_axis]] + spot[main_axis + 1:]
    return drawn.at[tuple(spot)].set(low).at[tuple(next_to)].set(top_value)


def steps_of(stream_key, dims, shards, least, largest):
    factor_of, own = 1.0, jax.random.fold_in(stream_key, 6)
    for axis_at, shards_of in shards:
        draws = jnp.exp(jax.random.uniform(jax.random.fold_in(own, axis_at), (shards_of,), jnp.float32, least / len(shards), largest / len(shards)))
        factor_of = factor_of * jnp.repeat(draws, dims[axis_at] // shards_of).reshape([-1 if axis == axis_at else 1 for axis in range(len(dims))])
    return factor_of


def bell_draw(own_key, shape, deviation, limit, split=(), held_as=jnp.bfloat16):
    factor_of = steps_of(own_key, shape, split, -0.22, 0.18) if split else 1.0
    values = jax.random.normal(own_key, shape, jnp.float32) * deviation * factor_of
    return jnp.minimum(jnp.maximum(values, -limit), limit).astype(held_as)


def setup_inputs(seed: int = 0) -> dict:
    splits = jax.random.split(jax.random.key(seed), 7)
    voltages = bell_draw(splits[0], (GROUPS, SUBANT, 2, SNAP, CHANS), 45.0, 270.0, ((0, 24), (1, 32)))
    source_flux = jnp.clip(jnp.exp(math.log(10.0) - 4.6051702 * jax.random.uniform(splits[1], (CHANS, SOURCES), jnp.float32) ** steps_of(splits[1], (CHANS, SOURCES), ((0, 32),), -0.2, 0.2)), 0.1, 10.0)
    initial_gains = bell_draw(splits[2], (CHANS, 2, GROUPS, SUBANT), 1.0, 4.0, ((0, 32), (2, 24)), jnp.float32)
    antenna_positions = jnp.clip(jax.random.uniform(splits[3], (2, GROUPS, SUBANT), jnp.float32, -1.0, 1.0), -1.0, 1.0)
    flagged = touch_ends((jax.random.randint(splits[4], (GROUPS, SUBANT), 0, 8) < 1).astype(jnp.int32), jax.random.fold_in(splits[4], 1), 0, 1)
    source_pixels = touch_ends(jax.random.randint(splits[5], (SOURCES, 2), 0, PIX), jax.random.fold_in(splits[5], 1), 0, PIX - 1).astype(jnp.int32)
    return {"voltages": voltages, "source_flux": source_flux, "initial_gains": initial_gains, "antenna_positions": antenna_positions, "flagged": flagged, "source_pixels": source_pixels}


phase_scale = 2.0 * math.pi * 8.0
small_eps = 1e-6


def sky_steering(positions, ell_coord, emm_coord, frequency):
    angle = phase_scale * frequency * (positions[0][:, None] * ell_coord[None, :] + positions[1][:, None] * emm_coord[None, :])
    return jnp.cos(angle).astype(jnp.bfloat16), (-jnp.sin(angle)).astype(jnp.bfloat16)


def reference(voltages, source_flux, initial_gains, antenna_positions, flagged, source_pixels):
    groups = voltages.shape[0]
    subant = voltages.shape[1]
    samples = voltages.shape[3]
    chans = voltages.shape[4]
    antennas = groups * subant
    volts = jnp.transpose(voltages.reshape(antennas, 2, samples, chans), (3, 0, 1, 2))
    gains_start = initial_gains.reshape(chans, 2, antennas)
    positions = antenna_positions.reshape(2, antennas)
    flag_vec = flagged.reshape(antennas)
    live = (1 - flag_vec).astype(jnp.float32)
    apart = 1.0 - jnp.eye(antennas, dtype=jnp.float32)
    keep = live[:, None] * apart
    pixel_float = source_pixels.astype(jnp.float32)
    ell_coord = (pixel_float[:, 0] - 0.5 * PIX) / PIX
    emm_coord = (pixel_float[:, 1] - 0.5 * PIX) / PIX
    frequencies = 1.0 + jnp.arange(chans).astype(jnp.float32) / chans
    highest = lax.Precision.HIGHEST

    def channel(inputs):
        volt, fluxes, frequency, gains = inputs
        left = volt.reshape(antennas, 2 * samples)
        swapped = jnp.concatenate([volt[:, 1], -volt[:, 0]], axis=1)
        vis_re = jnp.dot(left, left.T, preferred_element_type=jnp.float32) / samples
        vis_im = jnp.dot(swapped, left.T, preferred_element_type=jnp.float32) / samples
        steer_re, steer_im = sky_steering(positions, ell_coord, emm_coord, frequency)
        weight_re = (fluxes[None, :] * steer_re).astype(jnp.bfloat16)
        weight_im = (fluxes[None, :] * steer_im).astype(jnp.bfloat16)
        steer_both = jnp.concatenate([steer_re, steer_im], axis=1)
        steer_swap = jnp.concatenate([steer_im, -steer_re], axis=1)
        weight_both = jnp.concatenate([weight_re, weight_im], axis=1)
        model_re = jnp.dot(steer_both, weight_both.T, preferred_element_type=jnp.float32)
        model_im = jnp.dot(steer_swap, weight_both.T, preferred_element_type=jnp.float32)
        data_re = keep * (model_re * vis_re + model_im * vis_im)
        data_im = keep * (model_re * vis_im - model_im * vis_re)
        power = keep * (model_re * model_re + model_im * model_im)
        for iteration in range(ITERS):
            gain_re = gains[0]
            gain_im = gains[1]
            num_re = jnp.dot(gain_re, data_re, precision=highest) + jnp.dot(gain_im, data_im, precision=highest)
            num_im = jnp.dot(gain_re, data_im, precision=highest) - jnp.dot(gain_im, data_re, precision=highest)
            denominator = jnp.dot(gain_re * gain_re + gain_im * gain_im, power, precision=highest)
            fresh = jnp.stack([num_re / (denominator + small_eps), -num_im / (denominator + small_eps)])
            gains = jnp.where(flag_vec[None, :] == 1, gains, 0.5 * (gains + fresh))
        return gains

    result = lax.map(channel, (volts, source_flux, frequencies, gains_start))
    return result.reshape(chans, 2, groups, subant)
```

```python
import math

import jax
import jax.numpy as jnp
from jax import lax
from jax.sharding import PartitionSpec as P

PIX = 256
ITERS = 3


phase_scale = 2.0 * math.pi * 8.0
small_eps = 1e-06


def steering(positions, ell_coord, emm_coord, frequencies):
    angle = (
        phase_scale
        * frequencies[:, None, None]
        * (
            positions[0][None, :, None] * ell_coord[None, None, :]
            + positions[1][None, :, None] * emm_coord[None, None, :]
        )
    )
    return (jnp.cos(angle).astype(jnp.bfloat16), (-jnp.sin(angle)).astype(jnp.bfloat16))


def antenna_major(block):
    count, subant, halves, samples, chans = block.shape
    return jnp.transpose(block, (4, 0, 1, 2, 3)).reshape(chans, count * subant, halves, samples)


def on_device(voltages, source_flux, initial_gains, antenna_positions, flagged, source_pixels):
    n_rows = lax.axis_size("row")
    n_cols = lax.axis_size("col")
    n_chans = lax.axis_size("chan")
    row_index = lax.axis_index("row")
    col_index = lax.axis_index("col")
    chan_index = lax.axis_index("chan")
    groups, subant = antenna_positions.shape[1], antenna_positions.shape[2]
    antennas = groups * subant
    per_chan = source_flux.shape[0]
    samples = voltages.shape[3]
    own_group = row_index * n_cols + col_index

    own_volt = lax.all_to_all(voltages, "chan", split_axis=4, concat_axis=1, tiled=True)
    all_volt = lax.all_gather(own_volt, ("row", "col"), axis=0, tiled=True)
    all_gains = lax.all_gather(initial_gains, ("row", "col"), axis=2, tiled=True)

    q_antenna = antenna_major(all_volt)
    p_antenna = antenna_major(own_volt)
    q_left = q_antenna.reshape(per_chan, antennas, 2 * samples)
    q_swap = jnp.concatenate([q_antenna[:, :, 1], -q_antenna[:, :, 0]], axis=2)
    p_left = p_antenna.reshape(per_chan, subant, 2 * samples)
    vis_re = (
        jnp.einsum("cpk,cqk->cpq", p_left, q_left, preferred_element_type=jnp.float32) / samples
    )
    vis_im = (
        jnp.einsum("cpk,cqk->cpq", p_left, q_swap, preferred_element_type=jnp.float32) / samples
    )
    positions = antenna_positions.reshape(2, antennas)
    p_pos = lax.dynamic_index_in_dim(antenna_positions, own_group, 1, keepdims=False)
    flag_vec = flagged.reshape(antennas)
    own_flag = lax.dynamic_index_in_dim(flagged, own_group, 0, keepdims=False)
    q_ids = jnp.arange(antennas, dtype=jnp.int32)
    p_ids = own_group * subant + jnp.arange(subant, dtype=jnp.int32)
    pixel_float = source_pixels.astype(jnp.float32)
    ell_coord = (pixel_float[:, 0] - 0.5 * PIX) / PIX
    emm_coord = (pixel_float[:, 1] - 0.5 * PIX) / PIX
    channel_ids = chan_index * per_chan + jnp.arange(per_chan, dtype=jnp.int32)
    frequencies = 1.0 + channel_ids.astype(jnp.float32) / (per_chan * n_chans)
    steer_re, steer_im = steering(positions, ell_coord, emm_coord, frequencies)
    far_re, far_im = steering(p_pos, ell_coord, emm_coord, frequencies)
    weight_re = (source_flux[:, None, :] * far_re).astype(jnp.bfloat16)
    weight_im = (source_flux[:, None, :] * far_im).astype(jnp.bfloat16)
    steer_both = jnp.concatenate([steer_re, steer_im], axis=2)
    steer_swap = jnp.concatenate([steer_im, -steer_re], axis=2)
    weight_both = jnp.concatenate([weight_re, weight_im], axis=2)
    model_re = jnp.einsum(
        "cpk,cqk->cpq", weight_both, steer_both, preferred_element_type=jnp.float32
    )
    model_im = jnp.einsum(
        "cpk,cqk->cpq", weight_both, steer_swap, preferred_element_type=jnp.float32
    )
    live = (1 - flag_vec).astype(jnp.float32)
    apart = (p_ids[:, None] != q_ids[None, :]).astype(jnp.float32)
    keep = (live[None, :] * apart)[None, :, :]
    data_re = keep * (model_re * vis_re + model_im * vis_im)
    data_im = keep * (model_re * vis_im - model_im * vis_re)
    power = keep * (model_re * model_re + model_im * model_im)
    highest = lax.Precision.HIGHEST
    current = initial_gains[:, :, 0, :]
    gains_q = all_gains.reshape(per_chan, 2, antennas)
    for iteration in range(ITERS):
        if iteration > 0:
            gains_q = lax.all_gather(current, ("row", "col"), axis=2, tiled=True)
        gain_re = gains_q[:, 0]
        gain_im = gains_q[:, 1]
        num_re = jnp.einsum("cq,cpq->cp", gain_re, data_re, precision=highest) + jnp.einsum(
            "cq,cpq->cp", gain_im, data_im, precision=highest
        )
        num_im = jnp.einsum("cq,cpq->cp", gain_re, data_im, precision=highest) - jnp.einsum(
            "cq,cpq->cp", gain_im, data_re, precision=highest
        )
        denominator = jnp.einsum(
            "cq,cpq->cp", gain_re * gain_re + gain_im * gain_im, power, precision=highest
        )
        fresh = jnp.stack(
            [num_re / (denominator + small_eps), -num_im / (denominator + small_eps)], axis=1
        )
        current = jnp.where(own_flag[None, None, :] == 1, current, 0.5 * (current + fresh))
    return current[:, :, None, :]


def solution(mesh):
    in_specs = (
        P(("row", "col"), "chan", None, None, None),
        P("chan", None),
        P("chan", None, ("row", "col"), None),
        P(),
        P(),
        P(),
    )
    out_specs = P("chan", None, ("row", "col"), None)
    return jax.shard_map(
        on_device, mesh=mesh, in_specs=in_specs, out_specs=out_specs, check_vma=False
    )
```

```python
import math

import jax
import jax.numpy as jnp
from jax import lax
from jax.sharding import PartitionSpec as P

PIX = 256
ITERS = 3


phase_scale = 2.0 * math.pi * 8.0
small_eps = 1e-06


def steering(positions, ell_coord, emm_coord, frequencies):
    angle = (
        phase_scale
        * frequencies[:, None, None]
        * (
            positions[0][None, :, None] * ell_coord[None, None, :]
            + positions[1][None, :, None] * emm_coord[None, None, :]
        )
    )
    return (jnp.cos(angle).astype(jnp.bfloat16), (-jnp.sin(angle)).astype(jnp.bfloat16))


def antenna_major(block):
    count, subant, halves, samples, chans = block.shape
    return jnp.transpose(block, (4, 0, 1, 2, 3)).reshape(chans, count * subant, halves, samples)


def share(own_gains):
    n_cols = lax.axis_size("col")
    outgoing = jnp.broadcast_to(own_gains[None], (n_cols,) + own_gains.shape)
    gathered = lax.all_to_all(outgoing, "col", 0, 0, tiled=True)
    return jnp.transpose(gathered, (1, 2, 0, 3))


def on_device(voltages, source_flux, initial_gains, antenna_positions, flagged, source_pixels):
    n_rows = lax.axis_size("row")
    n_cols = lax.axis_size("col")
    n_chans = lax.axis_size("chan")
    row_index = lax.axis_index("row")
    col_index = lax.axis_index("col")
    chan_index = lax.axis_index("chan")
    subant = antenna_positions.shape[2]
    per_chan = source_flux.shape[0]
    samples = voltages.shape[3]
    row_pieces = lax.all_gather(voltages, "col", axis=0, tiled=True)
    col_pieces = lax.all_gather(voltages, "row", axis=0, tiled=True)
    row_volt, col_volt = (
        lax.all_to_all(row_pieces, "chan", split_axis=4, concat_axis=1, tiled=True),
        lax.all_to_all(col_pieces, "chan", split_axis=4, concat_axis=1, tiled=True),
    )
    row_antenna = antenna_major(row_volt)
    col_antenna = antenna_major(col_volt)
    row_count = row_antenna.shape[1]
    col_count = col_antenna.shape[1]
    row_left = row_antenna.reshape(per_chan, row_count, 2 * samples)
    row_swap = jnp.concatenate([row_antenna[:, :, 1], -row_antenna[:, :, 0]], axis=2)
    col_left = col_antenna.reshape(per_chan, col_count, 2 * samples)
    vis_re = (
        jnp.einsum("cqk,cpk->cqp", row_left, col_left, preferred_element_type=jnp.float32) / samples
    )
    vis_im = (
        jnp.einsum("cqk,cpk->cqp", row_swap, col_left, preferred_element_type=jnp.float32) / samples
    )
    row_pos = lax.dynamic_slice_in_dim(antenna_positions, row_index * n_cols, n_cols, 1).reshape(
        2, row_count
    )
    col_pos = lax.dynamic_index_in_dim(
        antenna_positions.reshape(2, n_rows, n_cols, subant), col_index, 2, keepdims=False
    ).reshape(2, col_count)
    row_flag = lax.dynamic_slice_in_dim(flagged, row_index * n_cols, n_cols, 0).reshape(row_count)
    own_flag = lax.dynamic_index_in_dim(flagged, row_index * n_cols + col_index, 0, keepdims=False)
    row_ids = row_index * n_cols * subant + jnp.arange(row_count, dtype=jnp.int32)
    col_ids = (
        (jnp.arange(n_rows, dtype=jnp.int32) * n_cols + col_index)[:, None] * subant
        + jnp.arange(subant, dtype=jnp.int32)[None, :]
    ).reshape(col_count)
    pixel_float = source_pixels.astype(jnp.float32)
    ell_coord = (pixel_float[:, 0] - 0.5 * PIX) / PIX
    emm_coord = (pixel_float[:, 1] - 0.5 * PIX) / PIX
    channel_ids = chan_index * per_chan + jnp.arange(per_chan, dtype=jnp.int32)
    frequencies = 1.0 + channel_ids.astype(jnp.float32) / (per_chan * n_chans)
    steer_re, steer_im = steering(row_pos, ell_coord, emm_coord, frequencies)
    far_re, far_im = steering(col_pos, ell_coord, emm_coord, frequencies)
    weight_re = (source_flux[:, None, :] * far_re).astype(jnp.bfloat16)
    weight_im = (source_flux[:, None, :] * far_im).astype(jnp.bfloat16)
    steer_both = jnp.concatenate([steer_re, steer_im], axis=2)
    steer_swap = jnp.concatenate([steer_im, -steer_re], axis=2)
    weight_both = jnp.concatenate([weight_re, weight_im], axis=2)
    model_re = jnp.einsum(
        "cqk,cpk->cqp", steer_both, weight_both, preferred_element_type=jnp.float32
    )
    model_im = jnp.einsum(
        "cqk,cpk->cqp", steer_swap, weight_both, preferred_element_type=jnp.float32
    )
    live = (1 - row_flag).astype(jnp.float32)
    apart = (row_ids[:, None] != col_ids[None, :]).astype(jnp.float32)
    keep = (live[:, None] * apart)[None, :, :]
    data_re = keep * (model_re * vis_re + model_im * vis_im)
    data_im = keep * (model_re * vis_im - model_im * vis_re)
    power = keep * (model_re * model_re + model_im * model_im)
    highest = lax.Precision.HIGHEST
    current = initial_gains[:, :, 0, :]
    row_flags = row_flag.reshape(1, 1, n_cols, subant)
    row_gains = share(current)
    for iteration in range(ITERS):
        gain_re = row_gains[:, 0].reshape(per_chan, row_count)
        gain_im = row_gains[:, 1].reshape(per_chan, row_count)
        num_re = jnp.einsum("cq,cqp->cp", gain_re, data_re, precision=highest) + jnp.einsum(
            "cq,cqp->cp", gain_im, data_im, precision=highest
        )
        num_im = jnp.einsum("cq,cqp->cp", gain_re, data_im, precision=highest) - jnp.einsum(
            "cq,cqp->cp", gain_im, data_re, precision=highest
        )
        denominator = jnp.einsum(
            "cq,cqp->cp", gain_re * gain_re + gain_im * gain_im, power, precision=highest
        )
        partial = jnp.stack([num_re, num_im, denominator], axis=0).reshape(3, per_chan, n_rows, subant)
        outgoing = jnp.broadcast_to(
            jnp.transpose(partial, (2, 0, 1, 3))[:, None], (n_rows, n_cols, 3, per_chan, subant)
        ).reshape(n_rows * n_cols, 3, per_chan, subant)
        incoming = lax.all_to_all(outgoing, ("row", "col"), 0, 0, tiled=True)
        totals = incoming.reshape(n_rows, n_cols, 3, per_chan, subant).sum(axis=0)
        total_re = jnp.transpose(totals[:, 0], (1, 0, 2))
        total_im = jnp.transpose(totals[:, 1], (1, 0, 2))
        total_den = jnp.transpose(totals[:, 2], (1, 0, 2))
        fresh = jnp.stack(
            [total_re / (total_den + small_eps), -total_im / (total_den + small_eps)], axis=1
        )
        row_gains = jnp.where(row_flags == 1, row_gains, 0.5 * (row_gains + fresh))
    current = lax.dynamic_index_in_dim(row_gains, col_index, 2, keepdims=False)
    return current[:, :, None, :]


def solution(mesh):
    in_specs = (
        P(("row", "col"), "chan", None, None, None),
        P("chan", None),
        P("chan", None, ("row", "col"), None),
        P(),
        P(),
        P(),
    )
    out_specs = P("chan", None, ("row", "col"), None)
    return jax.shard_map(
        on_device, mesh=mesh, in_specs=in_specs, out_specs=out_specs, check_vma=False
    )
```

```python
import math

import jax
import jax.numpy as jnp
from jax import lax
from jax.sharding import PartitionSpec as P

PIX = 256
ITERS = 3


phase_scale = 2.0 * math.pi * 8.0
small_eps = 1e-06


def steering(positions, ell_coord, emm_coord, frequencies):
    angle = (
        phase_scale
        * frequencies[:, None, None]
        * (
            positions[0][None, :, None] * ell_coord[None, None, :]
            + positions[1][None, :, None] * emm_coord[None, None, :]
        )
    )
    return (jnp.cos(angle).astype(jnp.bfloat16), (-jnp.sin(angle)).astype(jnp.bfloat16))


def antenna_major(block):
    count, subant, halves, samples, chans = block.shape
    return jnp.transpose(block, (4, 0, 1, 2, 3)).reshape(chans, count * subant, halves, samples)


def share(own_gains):
    n_cols = lax.axis_size("col")
    outgoing = jnp.broadcast_to(own_gains[None], (n_cols,) + own_gains.shape)
    gathered = lax.all_to_all(outgoing, "col", 0, 0, tiled=True)
    return jnp.transpose(gathered, (1, 2, 0, 3))


def gather_groups(block, axis):
    count = lax.axis_size(axis)
    outgoing = jnp.broadcast_to(block[None], (count,) + block.shape)
    gathered = lax.all_to_all(outgoing, axis, 0, 0, tiled=True)
    return gathered.reshape((count * block.shape[0],) + block.shape[1:])


def on_device(voltages, source_flux, initial_gains, antenna_positions, flagged, source_pixels):
    n_rows = lax.axis_size("row")
    n_cols = lax.axis_size("col")
    n_chans = lax.axis_size("chan")
    row_index = lax.axis_index("row")
    col_index = lax.axis_index("col")
    chan_index = lax.axis_index("chan")
    subant = antenna_positions.shape[2]
    per_chan = source_flux.shape[0]
    samples = voltages.shape[3]
    own_volt = lax.all_to_all(voltages, "chan", split_axis=4, concat_axis=1, tiled=True)
    row_volt = gather_groups(own_volt, "col")
    col_volt = gather_groups(own_volt, "row")
    row_antenna = antenna_major(row_volt)
    col_antenna = antenna_major(col_volt)
    row_count = row_antenna.shape[1]
    col_count = col_antenna.shape[1]
    row_left = row_antenna.reshape(per_chan, row_count, 2 * samples)
    row_swap = jnp.concatenate([row_antenna[:, :, 1], -row_antenna[:, :, 0]], axis=2)
    col_left = col_antenna.reshape(per_chan, col_count, 2 * samples)
    vis_re = (
        jnp.einsum("cqk,cpk->cqp", row_left, col_left, preferred_element_type=jnp.float32) / samples
    )
    vis_im = (
        jnp.einsum("cqk,cpk->cqp", row_swap, col_left, preferred_element_type=jnp.float32) / samples
    )
    row_pos = lax.dynamic_slice_in_dim(antenna_positions, row_index * n_cols, n_cols, 1).reshape(
        2, row_count
    )
    col_pos = lax.dynamic_index_in_dim(
        antenna_positions.reshape(2, n_rows, n_cols, subant), col_index, 2, keepdims=False
    ).reshape(2, col_count)
    row_flag = lax.dynamic_slice_in_dim(flagged, row_index * n_cols, n_cols, 0).reshape(row_count)
    own_flag = lax.dynamic_index_in_dim(flagged, row_index * n_cols + col_index, 0, keepdims=False)
    row_ids = row_index * n_cols * subant + jnp.arange(row_count, dtype=jnp.int32)
    col_ids = (
        (jnp.arange(n_rows, dtype=jnp.int32) * n_cols + col_index)[:, None] * subant
        + jnp.arange(subant, dtype=jnp.int32)[None, :]
    ).reshape(col_count)
    pixel_float = source_pixels.astype(jnp.float32)
    ell_coord = (pixel_float[:, 0] - 0.5 * PIX) / PIX
    emm_coord = (pixel_float[:, 1] - 0.5 * PIX) / PIX
    channel_ids = chan_index * per_chan + jnp.arange(per_chan, dtype=jnp.int32)
    frequencies = 1.0 + channel_ids.astype(jnp.float32) / (per_chan * n_chans)
    steer_re, steer_im = steering(row_pos, ell_coord, emm_coord, frequencies)
    far_re, far_im = steering(col_pos, ell_coord, emm_coord, frequencies)
    weight_re = (source_flux[:, None, :] * far_re).astype(jnp.bfloat16)
    weight_im = (source_flux[:, None, :] * far_im).astype(jnp.bfloat16)
    steer_both = jnp.concatenate([steer_re, steer_im], axis=2)
    steer_swap = jnp.concatenate([steer_im, -steer_re], axis=2)
    weight_both = jnp.concatenate([weight_re, weight_im], axis=2)
    model_re = jnp.einsum(
        "cqk,cpk->cqp", steer_both, weight_both, preferred_element_type=jnp.float32
    )
    model_im = jnp.einsum(
        "cqk,cpk->cqp", steer_swap, weight_both, preferred_element_type=jnp.float32
    )
    live = (1 - row_flag).astype(jnp.float32)
    apart = (row_ids[:, None] != col_ids[None, :]).astype(jnp.float32)
    keep = (live[:, None] * apart)[None, :, :]
    data_re = keep * (model_re * vis_re + model_im * vis_im)
    data_im = keep * (model_re * vis_im - model_im * vis_re)
    power = keep * (model_re * model_re + model_im * model_im)
    highest = lax.Precision.HIGHEST
    current = initial_gains[:, :, 0, :]
    row_flags = row_flag.reshape(1, 1, n_cols, subant)
    row_gains = share(current)
    for iteration in range(ITERS):
        gain_re = row_gains[:, 0].reshape(per_chan, row_count)
        gain_im = row_gains[:, 1].reshape(per_chan, row_count)
        num_re = jnp.einsum("cq,cqp->cp", gain_re, data_re, precision=highest) + jnp.einsum(
            "cq,cqp->cp", gain_im, data_im, precision=highest
        )
        num_im = jnp.einsum("cq,cqp->cp", gain_re, data_im, precision=highest) - jnp.einsum(
            "cq,cqp->cp", gain_im, data_re, precision=highest
        )
        denominator = jnp.einsum(
            "cq,cqp->cp", gain_re * gain_re + gain_im * gain_im, power, precision=highest
        )
        partial = jnp.stack([num_re, num_im, denominator], axis=0).reshape(3, per_chan, n_rows, subant)
        outgoing = jnp.broadcast_to(
            jnp.transpose(partial, (2, 0, 1, 3))[:, None], (n_rows, n_cols, 3, per_chan, subant)
        ).reshape(n_rows * n_cols, 3, per_chan, subant)
        incoming = lax.all_to_all(outgoing, ("row", "col"), 0, 0, tiled=True)
        totals = incoming.reshape(n_rows, n_cols, 3, per_chan, subant).sum(axis=0)
        total_re = jnp.transpose(totals[:, 0], (1, 0, 2))
        total_im = jnp.transpose(totals[:, 1], (1, 0, 2))
        total_den = jnp.transpose(totals[:, 2], (1, 0, 2))
        fresh = jnp.stack(
            [total_re / (total_den + small_eps), -total_im / (total_den + small_eps)], axis=1
        )
        row_gains = jnp.where(row_flags == 1, row_gains, 0.5 * (row_gains + fresh))
    current = lax.dynamic_index_in_dim(row_gains, col_index, 2, keepdims=False)
    return current[:, :, None, :]


def solution(mesh):
    in_specs = (
        P(("row", "col"), "chan", None, None, None),
        P("chan", None),
        P("chan", None, ("row", "col"), None),
        P(),
        P(),
        P(),
    )
    out_specs = P("chan", None, ("row", "col"), None)
    return jax.shard_map(
        on_device, mesh=mesh, in_specs=in_specs, out_specs=out_specs, check_vma=False
    )
```

```python
import math

import jax
import jax.numpy as jnp
from jax import lax
from jax.sharding import PartitionSpec as P

PIX = 256
ITERS = 3


phase_scale = 2.0 * math.pi * 8.0
small_eps = 1e-06


def steering(positions, ell_coord, emm_coord, frequencies):
    angle = (
        phase_scale
        * frequencies[:, None, None]
        * (
            positions[0][None, :, None] * ell_coord[None, None, :]
            + positions[1][None, :, None] * emm_coord[None, None, :]
        )
    )
    return (jnp.cos(angle).astype(jnp.bfloat16), (-jnp.sin(angle)).astype(jnp.bfloat16))


def antenna_major(block):
    count, subant, halves, samples, chans = block.shape
    return jnp.transpose(block, (4, 0, 1, 2, 3)).reshape(chans, count * subant, halves, samples)


def gather_groups(block, axis):
    count = lax.axis_size(axis)
    outgoing = jnp.broadcast_to(block[None], (count,) + block.shape)
    gathered = lax.all_to_all(outgoing, axis, 0, 0, tiled=True)
    return gathered.reshape((count * block.shape[0],) + block.shape[1:])


def on_device(voltages, source_flux, initial_gains, antenna_positions, flagged, source_pixels):
    n_rows = lax.axis_size("row")
    n_cols = lax.axis_size("col")
    n_chans = lax.axis_size("chan")
    row_index = lax.axis_index("row")
    col_index = lax.axis_index("col")
    chan_index = lax.axis_index("chan")
    subant = antenna_positions.shape[2]
    per_chan = source_flux.shape[0]
    samples = voltages.shape[3]
    own_volt = lax.all_to_all(voltages, "chan", split_axis=4, concat_axis=1, tiled=True)
    volt_size = own_volt.size
    row_both = gather_groups(
        jnp.concatenate(
            [own_volt.astype(jnp.float32).reshape(-1), initial_gains.reshape(-1)]
        )[None],
        "col",
    )
    row_volt = row_both[:, :volt_size].astype(jnp.bfloat16).reshape((n_cols,) + own_volt.shape[1:])
    col_volt = gather_groups(own_volt, "row")
    row_antenna = antenna_major(row_volt)
    col_antenna = antenna_major(col_volt)
    row_count = row_antenna.shape[1]
    col_count = col_antenna.shape[1]
    row_left = row_antenna.reshape(per_chan, row_count, 2 * samples)
    row_swap = jnp.concatenate([row_antenna[:, :, 1], -row_antenna[:, :, 0]], axis=2)
    col_left = col_antenna.reshape(per_chan, col_count, 2 * samples)
    vis_re = (
        jnp.einsum("cqk,cpk->cqp", row_left, col_left, preferred_element_type=jnp.float32) / samples
    )
    vis_im = (
        jnp.einsum("cqk,cpk->cqp", row_swap, col_left, preferred_element_type=jnp.float32) / samples
    )
    row_pos = lax.dynamic_slice_in_dim(antenna_positions, row_index * n_cols, n_cols, 1).reshape(
        2, row_count
    )
    col_pos = lax.dynamic_index_in_dim(
        antenna_positions.reshape(2, n_rows, n_cols, subant), col_index, 2, keepdims=False
    ).reshape(2, col_count)
    row_flag = lax.dynamic_slice_in_dim(flagged, row_index * n_cols, n_cols, 0).reshape(row_count)
    own_flag = lax.dynamic_index_in_dim(flagged, row_index * n_cols + col_index, 0, keepdims=False)
    row_ids = row_index * n_cols * subant + jnp.arange(row_count, dtype=jnp.int32)
    col_ids = (
        (jnp.arange(n_rows, dtype=jnp.int32) * n_cols + col_index)[:, None] * subant
        + jnp.arange(subant, dtype=jnp.int32)[None, :]
    ).reshape(col_count)
    pixel_float = source_pixels.astype(jnp.float32)
    ell_coord = (pixel_float[:, 0] - 0.5 * PIX) / PIX
    emm_coord = (pixel_float[:, 1] - 0.5 * PIX) / PIX
    channel_ids = chan_index * per_chan + jnp.arange(per_chan, dtype=jnp.int32)
    frequencies = 1.0 + channel_ids.astype(jnp.float32) / (per_chan * n_chans)
    steer_re, steer_im = steering(row_pos, ell_coord, emm_coord, frequencies)
    far_re, far_im = steering(col_pos, ell_coord, emm_coord, frequencies)
    weight_re = (source_flux[:, None, :] * far_re).astype(jnp.bfloat16)
    weight_im = (source_flux[:, None, :] * far_im).astype(jnp.bfloat16)
    steer_both = jnp.concatenate([steer_re, steer_im], axis=2)
    steer_swap = jnp.concatenate([steer_im, -steer_re], axis=2)
    weight_both = jnp.concatenate([weight_re, weight_im], axis=2)
    model_re = jnp.einsum(
        "cqk,cpk->cqp", steer_both, weight_both, preferred_element_type=jnp.float32
    )
    model_im = jnp.einsum(
        "cqk,cpk->cqp", steer_swap, weight_both, preferred_element_type=jnp.float32
    )
    live = (1 - row_flag).astype(jnp.float32)
    apart = (row_ids[:, None] != col_ids[None, :]).astype(jnp.float32)
    keep = (live[:, None] * apart)[None, :, :]
    data_re = keep * (model_re * vis_re + model_im * vis_im)
    data_im = keep * (model_re * vis_im - model_im * vis_re)
    power = keep * (model_re * model_re + model_im * model_im)
    highest = lax.Precision.HIGHEST
    row_flags = row_flag.reshape(1, 1, n_cols, subant)
    row_gains = jnp.transpose(row_both[:, volt_size:].reshape(n_cols, per_chan, 2, subant), (1, 2, 0, 3))
    for iteration in range(ITERS):
        gain_re = row_gains[:, 0].reshape(per_chan, row_count)
        gain_im = row_gains[:, 1].reshape(per_chan, row_count)
        num_re = jnp.einsum("cq,cqp->cp", gain_re, data_re, precision=highest) + jnp.einsum(
            "cq,cqp->cp", gain_im, data_im, precision=highest
        )
        num_im = jnp.einsum("cq,cqp->cp", gain_re, data_im, precision=highest) - jnp.einsum(
            "cq,cqp->cp", gain_im, data_re, precision=highest
        )
        denominator = jnp.einsum(
            "cq,cqp->cp", gain_re * gain_re + gain_im * gain_im, power, precision=highest
        )
        partial = jnp.stack([num_re, num_im, denominator], axis=0).reshape(3, per_chan, n_rows, subant)
        partial = jnp.transpose(partial, (2, 0, 1, 3))
        if iteration == ITERS - 1:
            incoming = lax.all_to_all(partial, "row", 0, 0, tiled=True)
            own_totals = incoming.sum(axis=0)
            fresh = jnp.stack(
                [
                    own_totals[0] / (own_totals[2] + small_eps),
                    -own_totals[1] / (own_totals[2] + small_eps),
                ],
                axis=1,
            )
            current = lax.dynamic_index_in_dim(row_gains, col_index, 2, keepdims=False)
            current = jnp.where(own_flag[None, None, :] == 1, current, 0.5 * (current + fresh))
            break
        outgoing = jnp.broadcast_to(
            partial[:, None], (n_rows, n_cols, 3, per_chan, subant)
        ).reshape(n_rows * n_cols, 3, per_chan, subant)
        incoming = lax.all_to_all(outgoing, ("row", "col"), 0, 0, tiled=True)
        totals = incoming.reshape(n_rows, n_cols, 3, per_chan, subant).sum(axis=0)
        total_re = jnp.transpose(totals[:, 0], (1, 0, 2))
        total_im = jnp.transpose(totals[:, 1], (1, 0, 2))
        total_den = jnp.transpose(totals[:, 2], (1, 0, 2))
        fresh = jnp.stack(
            [total_re / (total_den + small_eps), -total_im / (total_den + small_eps)], axis=1
        )
        row_gains = jnp.where(row_flags == 1, row_gains, 0.5 * (row_gains + fresh))
    return current[:, :, None, :]


def solution(mesh):
    in_specs = (
        P(("row", "col"), "chan", None, None, None),
        P("chan", None),
        P("chan", None, ("row", "col"), None),
        P(),
        P(),
        P(),
    )
    out_specs = P("chan", None, ("row", "col"), None)
    return jax.shard_map(
        on_device, mesh=mesh, in_specs=in_specs, out_specs=out_specs, check_vma=False
    )
```

```python
import math

import jax
import jax.numpy as jnp
from jax import lax
from jax.sharding import PartitionSpec as P

PIX = 256
ITERS = 3


phase_scale = 2.0 * math.pi * 8.0
small_eps = 1e-06


def steering(positions, ell_coord, emm_coord, frequencies):
    angle = (
        phase_scale
        * frequencies[:, None, None]
        * (
            positions[0][None, :, None] * ell_coord[None, None, :]
            + positions[1][None, :, None] * emm_coord[None, None, :]
        )
    )
    return (jnp.cos(angle).astype(jnp.bfloat16), (-jnp.sin(angle)).astype(jnp.bfloat16))


def antenna_major(block):
    count, subant, halves, samples, chans = block.shape
    return jnp.transpose(block, (4, 0, 1, 2, 3)).reshape(chans, count * subant, halves, samples)


def gather_groups(block, axis):
    count = lax.axis_size(axis)
    outgoing = jnp.broadcast_to(block[None], (count,) + block.shape)
    gathered = lax.all_to_all(outgoing, axis, 0, 0, tiled=True)
    return gathered.reshape((count * block.shape[0],) + block.shape[1:])


def gather_by_shifts(block, axis):
    count = lax.axis_size(axis)
    index = lax.axis_index(axis)
    pieces = [block]
    for shift in range(1, count):
        pieces.append(lax.ppermute(block, axis, [(i, (i + shift) % count) for i in range(count)]))
    stacked = jnp.concatenate(pieces, axis=0)
    order = (index - jnp.arange(count, dtype=jnp.int32)) % count
    return jnp.take(stacked, order, axis=0)


def on_device(voltages, source_flux, initial_gains, antenna_positions, flagged, source_pixels):
    n_rows = lax.axis_size("row")
    n_cols = lax.axis_size("col")
    n_chans = lax.axis_size("chan")
    row_index = lax.axis_index("row")
    col_index = lax.axis_index("col")
    chan_index = lax.axis_index("chan")
    subant = antenna_positions.shape[2]
    per_chan = source_flux.shape[0]
    samples = voltages.shape[3]
    own_volt = lax.all_to_all(voltages, "chan", split_axis=4, concat_axis=1, tiled=True)
    volt_size = own_volt.size
    row_both = gather_by_shifts(
        jnp.concatenate(
            [own_volt.astype(jnp.float32).reshape(-1), initial_gains.reshape(-1)]
        )[None],
        "col",
    )
    row_volt = row_both[:, :volt_size].astype(jnp.bfloat16).reshape((n_cols,) + own_volt.shape[1:])
    col_volt = gather_by_shifts(own_volt, "row")
    row_antenna = antenna_major(row_volt)
    col_antenna = antenna_major(col_volt)
    row_count = row_antenna.shape[1]
    col_count = col_antenna.shape[1]
    row_left = row_antenna.reshape(per_chan, row_count, 2 * samples)
    row_swap = jnp.concatenate([row_antenna[:, :, 1], -row_antenna[:, :, 0]], axis=2)
    col_left = col_antenna.reshape(per_chan, col_count, 2 * samples)
    vis_re = (
        jnp.einsum("cqk,cpk->cqp", row_left, col_left, preferred_element_type=jnp.float32) / samples
    )
    vis_im = (
        jnp.einsum("cqk,cpk->cqp", row_swap, col_left, preferred_element_type=jnp.float32) / samples
    )
    row_pos = lax.dynamic_slice_in_dim(antenna_positions, row_index * n_cols, n_cols, 1).reshape(
        2, row_count
    )
    col_pos = lax.dynamic_index_in_dim(
        antenna_positions.reshape(2, n_rows, n_cols, subant), col_index, 2, keepdims=False
    ).reshape(2, col_count)
    row_flag = lax.dynamic_slice_in_dim(flagged, row_index * n_cols, n_cols, 0).reshape(row_count)
    own_flag = lax.dynamic_index_in_dim(flagged, row_index * n_cols + col_index, 0, keepdims=False)
    row_ids = row_index * n_cols * subant + jnp.arange(row_count, dtype=jnp.int32)
    col_ids = (
        (jnp.arange(n_rows, dtype=jnp.int32) * n_cols + col_index)[:, None] * subant
        + jnp.arange(subant, dtype=jnp.int32)[None, :]
    ).reshape(col_count)
    pixel_float = source_pixels.astype(jnp.float32)
    ell_coord = (pixel_float[:, 0] - 0.5 * PIX) / PIX
    emm_coord = (pixel_float[:, 1] - 0.5 * PIX) / PIX
    channel_ids = chan_index * per_chan + jnp.arange(per_chan, dtype=jnp.int32)
    frequencies = 1.0 + channel_ids.astype(jnp.float32) / (per_chan * n_chans)
    steer_re, steer_im = steering(row_pos, ell_coord, emm_coord, frequencies)
    far_re, far_im = steering(col_pos, ell_coord, emm_coord, frequencies)
    weight_re = (source_flux[:, None, :] * far_re).astype(jnp.bfloat16)
    weight_im = (source_flux[:, None, :] * far_im).astype(jnp.bfloat16)
    steer_both = jnp.concatenate([steer_re, steer_im], axis=2)
    steer_swap = jnp.concatenate([steer_im, -steer_re], axis=2)
    weight_both = jnp.concatenate([weight_re, weight_im], axis=2)
    model_re = jnp.einsum(
        "cqk,cpk->cqp", steer_both, weight_both, preferred_element_type=jnp.float32
    )
    model_im = jnp.einsum(
        "cqk,cpk->cqp", steer_swap, weight_both, preferred_element_type=jnp.float32
    )
    live = (1 - row_flag).astype(jnp.float32)
    apart = (row_ids[:, None] != col_ids[None, :]).astype(jnp.float32)
    keep = (live[:, None] * apart)[None, :, :]
    data_re = keep * (model_re * vis_re + model_im * vis_im)
    data_im = keep * (model_re * vis_im - model_im * vis_re)
    power = keep * (model_re * model_re + model_im * model_im)
    highest = lax.Precision.HIGHEST
    row_flags = row_flag.reshape(1, 1, n_cols, subant)
    row_gains = jnp.transpose(row_both[:, volt_size:].reshape(n_cols, per_chan, 2, subant), (1, 2, 0, 3))
    for iteration in range(ITERS):
        gain_re = row_gains[:, 0].reshape(per_chan, row_count)
        gain_im = row_gains[:, 1].reshape(per_chan, row_count)
        num_re = jnp.einsum("cq,cqp->cp", gain_re, data_re, precision=highest) + jnp.einsum(
            "cq,cqp->cp", gain_im, data_im, precision=highest
        )
        num_im = jnp.einsum("cq,cqp->cp", gain_re, data_im, precision=highest) - jnp.einsum(
            "cq,cqp->cp", gain_im, data_re, precision=highest
        )
        denominator = jnp.einsum(
            "cq,cqp->cp", gain_re * gain_re + gain_im * gain_im, power, precision=highest
        )
        partial = jnp.stack([num_re, num_im, denominator], axis=0).reshape(3, per_chan, n_rows, subant)
        partial = jnp.transpose(partial, (2, 0, 1, 3))
        if iteration == ITERS - 1:
            incoming = lax.all_to_all(partial, "row", 0, 0, tiled=True)
            own_totals = incoming.sum(axis=0)
            fresh = jnp.stack(
                [
                    own_totals[0] / (own_totals[2] + small_eps),
                    -own_totals[1] / (own_totals[2] + small_eps),
                ],
                axis=1,
            )
            current = lax.dynamic_index_in_dim(row_gains, col_index, 2, keepdims=False)
            current = jnp.where(own_flag[None, None, :] == 1, current, 0.5 * (current + fresh))
            break
        outgoing = jnp.broadcast_to(
            partial[:, None], (n_rows, n_cols, 3, per_chan, subant)
        ).reshape(n_rows * n_cols, 3, per_chan, subant)
        incoming = lax.all_to_all(outgoing, ("row", "col"), 0, 0, tiled=True)
        totals = incoming.reshape(n_rows, n_cols, 3, per_chan, subant).sum(axis=0)
        total_re = jnp.transpose(totals[:, 0], (1, 0, 2))
        total_im = jnp.transpose(totals[:, 1], (1, 0, 2))
        total_den = jnp.transpose(totals[:, 2], (1, 0, 2))
        fresh = jnp.stack(
            [total_re / (total_den + small_eps), -total_im / (total_den + small_eps)], axis=1
        )
        row_gains = jnp.where(row_flags == 1, row_gains, 0.5 * (row_gains + fresh))
    return current[:, :, None, :]


def solution(mesh):
    in_specs = (
        P(("row", "col"), "chan", None, None, None),
        P("chan", None),
        P("chan", None, ("row", "col"), None),
        P(),
        P(),
        P(),
    )
    out_specs = P("chan", None, ("row", "col"), None)
    return jax.shard_map(
        on_device, mesh=mesh, in_specs=in_specs, out_specs=out_specs, check_vma=False
    )
```

```python
import math

import jax
import jax.numpy as jnp
from jax import lax
from jax.sharding import PartitionSpec as P

PIX = 256
ITERS = 3


phase_scale = 2.0 * math.pi * 8.0
small_eps = 1e-06


def steering(positions, ell_coord, emm_coord, frequencies):
    angle = (
        phase_scale
        * frequencies[:, None, None]
        * (
            positions[0][None, :, None] * ell_coord[None, None, :]
            + positions[1][None, :, None] * emm_coord[None, None, :]
        )
    )
    return (jnp.cos(angle).astype(jnp.bfloat16), (-jnp.sin(angle)).astype(jnp.bfloat16))


def antenna_major(block):
    count, subant, halves, samples, chans = block.shape
    return jnp.transpose(block, (4, 0, 1, 2, 3)).reshape(chans, count * subant, halves, samples)


def gather_groups(block, axis):
    count = lax.axis_size(axis)
    outgoing = jnp.broadcast_to(block[None], (count,) + block.shape)
    gathered = lax.all_to_all(outgoing, axis, 0, 0, tiled=True)
    return gathered.reshape((count * block.shape[0],) + block.shape[1:])


def on_device(voltages, source_flux, initial_gains, antenna_positions, flagged, source_pixels):
    n_rows = lax.axis_size("row")
    n_cols = lax.axis_size("col")
    n_chans = lax.axis_size("chan")
    row_index = lax.axis_index("row")
    col_index = lax.axis_index("col")
    chan_index = lax.axis_index("chan")
    subant = antenna_positions.shape[2]
    per_chan = source_flux.shape[0]
    samples = voltages.shape[3]
    own_volt = lax.all_to_all(voltages, "chan", split_axis=4, concat_axis=1, tiled=True)
    volt_size = own_volt.size
    gains_flat = initial_gains.reshape(-1)
    gains_hi = lax.reduce_precision(gains_flat, exponent_bits=8, mantissa_bits=7)
    gains_rest = gains_flat - gains_hi
    gains_mid = lax.reduce_precision(gains_rest, exponent_bits=8, mantissa_bits=7)
    gains_lo = gains_rest - gains_mid
    gains_parts = jnp.stack([gains_hi, gains_mid, gains_lo]).astype(jnp.bfloat16).reshape(-1)
    row_both = gather_groups(jnp.concatenate([own_volt.reshape(-1), gains_parts])[None], "col")
    row_volt = row_both[:, :volt_size].reshape((n_cols,) + own_volt.shape[1:])
    col_volt = gather_groups(own_volt, "row")
    row_antenna = antenna_major(row_volt)
    col_antenna = antenna_major(col_volt)
    row_count = row_antenna.shape[1]
    col_count = col_antenna.shape[1]
    row_left = row_antenna.reshape(per_chan, row_count, 2 * samples)
    row_swap = jnp.concatenate([row_antenna[:, :, 1], -row_antenna[:, :, 0]], axis=2)
    col_left = col_antenna.reshape(per_chan, col_count, 2 * samples)
    vis_re = (
        jnp.einsum("cqk,cpk->cqp", row_left, col_left, preferred_element_type=jnp.float32) / samples
    )
    vis_im = (
        jnp.einsum("cqk,cpk->cqp", row_swap, col_left, preferred_element_type=jnp.float32) / samples
    )
    row_pos = lax.dynamic_slice_in_dim(antenna_positions, row_index * n_cols, n_cols, 1).reshape(
        2, row_count
    )
    col_pos = lax.dynamic_index_in_dim(
        antenna_positions.reshape(2, n_rows, n_cols, subant), col_index, 2, keepdims=False
    ).reshape(2, col_count)
    row_flag = lax.dynamic_slice_in_dim(flagged, row_index * n_cols, n_cols, 0).reshape(row_count)
    own_flag = lax.dynamic_index_in_dim(flagged, row_index * n_cols + col_index, 0, keepdims=False)
    row_ids = row_index * n_cols * subant + jnp.arange(row_count, dtype=jnp.int32)
    col_ids = (
        (jnp.arange(n_rows, dtype=jnp.int32) * n_cols + col_index)[:, None] * subant
        + jnp.arange(subant, dtype=jnp.int32)[None, :]
    ).reshape(col_count)
    pixel_float = source_pixels.astype(jnp.float32)
    ell_coord = (pixel_float[:, 0] - 0.5 * PIX) / PIX
    emm_coord = (pixel_float[:, 1] - 0.5 * PIX) / PIX
    channel_ids = chan_index * per_chan + jnp.arange(per_chan, dtype=jnp.int32)
    frequencies = 1.0 + channel_ids.astype(jnp.float32) / (per_chan * n_chans)
    steer_re, steer_im = steering(row_pos, ell_coord, emm_coord, frequencies)
    far_re, far_im = steering(col_pos, ell_coord, emm_coord, frequencies)
    weight_re = (source_flux[:, None, :] * far_re).astype(jnp.bfloat16)
    weight_im = (source_flux[:, None, :] * far_im).astype(jnp.bfloat16)
    steer_both = jnp.concatenate([steer_re, steer_im], axis=2)
    steer_swap = jnp.concatenate([steer_im, -steer_re], axis=2)
    weight_both = jnp.concatenate([weight_re, weight_im], axis=2)
    model_re = jnp.einsum(
        "cqk,cpk->cqp", steer_both, weight_both, preferred_element_type=jnp.float32
    )
    model_im = jnp.einsum(
        "cqk,cpk->cqp", steer_swap, weight_both, preferred_element_type=jnp.float32
    )
    live = (1 - row_flag).astype(jnp.float32)
    apart = (row_ids[:, None] != col_ids[None, :]).astype(jnp.float32)
    keep = (live[:, None] * apart)[None, :, :]
    data_re = keep * (model_re * vis_re + model_im * vis_im)
    data_im = keep * (model_re * vis_im - model_im * vis_re)
    power = keep * (model_re * model_re + model_im * model_im)
    highest = lax.Precision.HIGHEST
    row_flags = row_flag.reshape(1, 1, n_cols, subant)
    parts = row_both[:, volt_size:].astype(jnp.float32).reshape(n_cols, 3, per_chan, 2, subant)
    row_gains = jnp.transpose((parts[:, 0] + parts[:, 1]) + parts[:, 2], (1, 2, 0, 3))
    stacked_data = jnp.concatenate([data_re, data_im, power], axis=2)
    for iteration in range(ITERS):
        gain_re = row_gains[:, 0].reshape(per_chan, row_count)
        gain_im = row_gains[:, 1].reshape(per_chan, row_count)
        weights = jnp.stack([gain_re, gain_im, gain_re * gain_re + gain_im * gain_im], axis=1)
        products = jnp.einsum("ckq,cqm->ckm", weights, stacked_data, precision=highest)
        num_re = products[:, 0, :col_count] + products[:, 1, col_count : 2 * col_count]
        num_im = products[:, 0, col_count : 2 * col_count] - products[:, 1, :col_count]
        denominator = products[:, 2, 2 * col_count :]
        partial = jnp.stack([num_re, num_im, denominator], axis=0).reshape(3, per_chan, n_rows, subant)
        partial = jnp.transpose(partial, (2, 0, 1, 3))
        if iteration == ITERS - 1:
            incoming = lax.all_to_all(partial, "row", 0, 0, tiled=True)
            own_totals = incoming.sum(axis=0)
            fresh = jnp.stack(
                [
                    own_totals[0] / (own_totals[2] + small_eps),
                    -own_totals[1] / (own_totals[2] + small_eps),
                ],
                axis=1,
            )
            current = lax.dynamic_index_in_dim(row_gains, col_index, 2, keepdims=False)
            current = jnp.where(own_flag[None, None, :] == 1, current, 0.5 * (current + fresh))
            break
        outgoing = jnp.broadcast_to(
            partial[:, None], (n_rows, n_cols, 3, per_chan, subant)
        ).reshape(n_rows * n_cols, 3, per_chan, subant)
        incoming = lax.all_to_all(outgoing, ("row", "col"), 0, 0, tiled=True)
        totals = incoming.reshape(n_rows, n_cols, 3, per_chan, subant).sum(axis=0)
        total_re = jnp.transpose(totals[:, 0], (1, 0, 2))
        total_im = jnp.transpose(totals[:, 1], (1, 0, 2))
        total_den = jnp.transpose(totals[:, 2], (1, 0, 2))
        fresh = jnp.stack(
            [total_re / (total_den + small_eps), -total_im / (total_den + small_eps)], axis=1
        )
        row_gains = jnp.where(row_flags == 1, row_gains, 0.5 * (row_gains + fresh))
    return current[:, :, None, :]


def solution(mesh):
    in_specs = (
        P(("row", "col"), "chan", None, None, None),
        P("chan", None),
        P("chan", None, ("row", "col"), None),
        P(),
        P(),
        P(),
    )
    out_specs = P("chan", None, ("row", "col"), None)
    return jax.shard_map(
        on_device, mesh=mesh, in_specs=in_specs, out_specs=out_specs, check_vma=False
    )
```

```python
import math

import jax
import jax.numpy as jnp
from jax import lax
from jax.sharding import PartitionSpec as P

PIX = 256
ITERS = 3


phase_scale = 2.0 * math.pi * 8.0
small_eps = 1e-06


def steering(positions, ell_coord, emm_coord, frequencies):
    angle = (
        phase_scale
        * frequencies[:, None, None]
        * (
            positions[0][None, :, None] * ell_coord[None, None, :]
            + positions[1][None, :, None] * emm_coord[None, None, :]
        )
    )
    return (jnp.cos(angle).astype(jnp.bfloat16), (-jnp.sin(angle)).astype(jnp.bfloat16))


def gather_groups(block, axis):
    count = lax.axis_size(axis)
    outgoing = jnp.broadcast_to(block[:, None, :], (block.shape[0], count, block.shape[1]))
    return lax.all_to_all(outgoing, axis, 1, 1, tiled=True)


def on_device(voltages, source_flux, initial_gains, antenna_positions, flagged, source_pixels):
    n_rows = lax.axis_size("row")
    n_cols = lax.axis_size("col")
    n_chans = lax.axis_size("chan")
    row_index = lax.axis_index("row")
    col_index = lax.axis_index("col")
    chan_index = lax.axis_index("chan")
    subant = antenna_positions.shape[2]
    per_chan = source_flux.shape[0]
    samples = voltages.shape[3]
    count, own_ants, halves, _, all_chans = voltages.shape
    width = halves * samples
    local = jnp.transpose(voltages, (4, 0, 1, 2, 3)).reshape(all_chans, count * own_ants, width)
    own_volt = lax.all_to_all(local, "chan", split_axis=0, concat_axis=1, tiled=True)
    own_volt = own_volt.reshape(per_chan, subant * width)
    volt_size = subant * width
    gains_flat = initial_gains.reshape(per_chan, -1)
    gains_hi = lax.reduce_precision(gains_flat, exponent_bits=8, mantissa_bits=7)
    gains_rest = gains_flat - gains_hi
    gains_mid = lax.reduce_precision(gains_rest, exponent_bits=8, mantissa_bits=7)
    gains_lo = gains_rest - gains_mid
    gains_parts = jnp.stack([gains_hi, gains_mid, gains_lo], axis=1).astype(jnp.bfloat16)
    gains_parts = gains_parts.reshape(per_chan, -1)
    row_both = gather_groups(jnp.concatenate([own_volt, gains_parts], axis=1), "col")
    row_count = n_cols * subant
    col_count = n_rows * subant
    row_left = row_both[:, :, :volt_size].reshape(per_chan, row_count, width)
    col_left = gather_groups(own_volt, "row").reshape(per_chan, col_count, width)
    row_swap = jnp.concatenate([row_left[:, :, samples:], -row_left[:, :, :samples]], axis=2)
    vis_re = (
        jnp.einsum("cqk,cpk->cqp", row_left, col_left, preferred_element_type=jnp.float32) / samples
    )
    vis_im = (
        jnp.einsum("cqk,cpk->cqp", row_swap, col_left, preferred_element_type=jnp.float32) / samples
    )
    row_pos = lax.dynamic_slice_in_dim(antenna_positions, row_index * n_cols, n_cols, 1).reshape(
        2, row_count
    )
    col_pos = lax.dynamic_index_in_dim(
        antenna_positions.reshape(2, n_rows, n_cols, subant), col_index, 2, keepdims=False
    ).reshape(2, col_count)
    row_flag = lax.dynamic_slice_in_dim(flagged, row_index * n_cols, n_cols, 0).reshape(row_count)
    own_flag = lax.dynamic_index_in_dim(flagged, row_index * n_cols + col_index, 0, keepdims=False)
    row_ids = row_index * n_cols * subant + jnp.arange(row_count, dtype=jnp.int32)
    col_ids = (
        (jnp.arange(n_rows, dtype=jnp.int32) * n_cols + col_index)[:, None] * subant
        + jnp.arange(subant, dtype=jnp.int32)[None, :]
    ).reshape(col_count)
    pixel_float = source_pixels.astype(jnp.float32)
    ell_coord = (pixel_float[:, 0] - 0.5 * PIX) / PIX
    emm_coord = (pixel_float[:, 1] - 0.5 * PIX) / PIX
    channel_ids = chan_index * per_chan + jnp.arange(per_chan, dtype=jnp.int32)
    frequencies = 1.0 + channel_ids.astype(jnp.float32) / (per_chan * n_chans)
    steer_re, steer_im = steering(row_pos, ell_coord, emm_coord, frequencies)
    far_re, far_im = steering(col_pos, ell_coord, emm_coord, frequencies)
    weight_re = (source_flux[:, None, :] * far_re).astype(jnp.bfloat16)
    weight_im = (source_flux[:, None, :] * far_im).astype(jnp.bfloat16)
    steer_both = jnp.concatenate([steer_re, steer_im], axis=2)
    steer_swap = jnp.concatenate([steer_im, -steer_re], axis=2)
    weight_both = jnp.concatenate([weight_re, weight_im], axis=2)
    model_re = jnp.einsum(
        "cqk,cpk->cqp", steer_both, weight_both, preferred_element_type=jnp.float32
    )
    model_im = jnp.einsum(
        "cqk,cpk->cqp", steer_swap, weight_both, preferred_element_type=jnp.float32
    )
    live = (1 - row_flag).astype(jnp.float32)
    apart = (row_ids[:, None] != col_ids[None, :]).astype(jnp.float32)
    keep = (live[:, None] * apart)[None, :, :]
    data_re = keep * (model_re * vis_re + model_im * vis_im)
    data_im = keep * (model_re * vis_im - model_im * vis_re)
    power = keep * (model_re * model_re + model_im * model_im)
    highest = lax.Precision.HIGHEST
    row_flags = row_flag.reshape(1, 1, n_cols, subant)
    parts = row_both[:, :, volt_size:].astype(jnp.float32).reshape(per_chan, n_cols, 3, 2, subant)
    row_gains = jnp.transpose((parts[:, :, 0] + parts[:, :, 1]) + parts[:, :, 2], (0, 2, 1, 3))
    stacked_data = jnp.concatenate([data_re, data_im, power], axis=2)
    for iteration in range(ITERS):
        gain_re = row_gains[:, 0].reshape(per_chan, row_count)
        gain_im = row_gains[:, 1].reshape(per_chan, row_count)
        weights = jnp.stack([gain_re, gain_im, gain_re * gain_re + gain_im * gain_im], axis=1)
        products = jnp.einsum("ckq,cqm->ckm", weights, stacked_data, precision=highest)
        num_re = products[:, 0, :col_count] + products[:, 1, col_count : 2 * col_count]
        num_im = products[:, 0, col_count : 2 * col_count] - products[:, 1, :col_count]
        denominator = products[:, 2, 2 * col_count :]
        partial = jnp.stack([num_re, num_im, denominator], axis=0).reshape(3, per_chan, n_rows, subant)
        partial = jnp.transpose(partial, (2, 0, 1, 3))
        if iteration == ITERS - 1:
            incoming = lax.all_to_all(partial, "row", 0, 0, tiled=True)
            own_totals = incoming.sum(axis=0)
            fresh = jnp.stack(
                [
                    own_totals[0] / (own_totals[2] + small_eps),
                    -own_totals[1] / (own_totals[2] + small_eps),
                ],
                axis=1,
            )
            current = lax.dynamic_index_in_dim(row_gains, col_index, 2, keepdims=False)
            current = jnp.where(own_flag[None, None, :] == 1, current, 0.5 * (current + fresh))
            break
        outgoing = jnp.broadcast_to(
            partial[:, None], (n_rows, n_cols, 3, per_chan, subant)
        ).reshape(n_rows * n_cols, 3, per_chan, subant)
        incoming = lax.all_to_all(outgoing, ("row", "col"), 0, 0, tiled=True)
        totals = incoming.reshape(n_rows, n_cols, 3, per_chan, subant).sum(axis=0)
        total_re = jnp.transpose(totals[:, 0], (1, 0, 2))
        total_im = jnp.transpose(totals[:, 1], (1, 0, 2))
        total_den = jnp.transpose(totals[:, 2], (1, 0, 2))
        fresh = jnp.stack(
            [total_re / (total_den + small_eps), -total_im / (total_den + small_eps)], axis=1
        )
        row_gains = jnp.where(row_flags == 1, row_gains, 0.5 * (row_gains + fresh))
    return current[:, :, None, :]


def solution(mesh):
    in_specs = (
        P(("row", "col"), "chan", None, None, None),
        P("chan", None),
        P("chan", None, ("row", "col"), None),
        P(),
        P(),
        P(),
    )
    out_specs = P("chan", None, ("row", "col"), None)
    return jax.shard_map(
        on_device, mesh=mesh, in_specs=in_specs, out_specs=out_specs, check_vma=False
    )
```

```python
import math

import jax
import jax.numpy as jnp
from jax import lax
from jax.sharding import PartitionSpec as P

PIX = 256
ITERS = 3


phase_scale = 2.0 * math.pi * 8.0
small_eps = 1e-06


def steering(positions, ell_coord, emm_coord, frequencies):
    angle = (
        phase_scale
        * frequencies[:, None, None]
        * (
            positions[0][None, :, None] * ell_coord[None, None, :]
            + positions[1][None, :, None] * emm_coord[None, None, :]
        )
    )
    return (jnp.cos(angle).astype(jnp.bfloat16), (-jnp.sin(angle)).astype(jnp.bfloat16))


def gather_groups(block, axis):
    count = lax.axis_size(axis)
    outgoing = jnp.broadcast_to(block[:, None, :], (block.shape[0], count, block.shape[1]))
    return lax.all_to_all(outgoing, axis, 1, 1, tiled=True)


def on_device(voltages, source_flux, initial_gains, antenna_positions, flagged, source_pixels):
    n_rows = lax.axis_size("row")
    n_cols = lax.axis_size("col")
    n_chans = lax.axis_size("chan")
    row_index = lax.axis_index("row")
    col_index = lax.axis_index("col")
    chan_index = lax.axis_index("chan")
    subant = antenna_positions.shape[2]
    per_chan = source_flux.shape[0]
    samples = voltages.shape[3]
    count, own_ants, halves, _, all_chans = voltages.shape
    width = halves * samples
    local = jnp.transpose(voltages, (4, 0, 1, 2, 3)).reshape(all_chans, count * own_ants, width)
    own_volt = lax.all_to_all(local, "chan", split_axis=0, concat_axis=1, tiled=True)
    own_volt = own_volt.reshape(per_chan, subant * width)
    volt_size = subant * width
    gains_flat = initial_gains.reshape(per_chan, -1)
    gains_hi = lax.reduce_precision(gains_flat, exponent_bits=8, mantissa_bits=7)
    gains_rest = gains_flat - gains_hi
    gains_mid = lax.reduce_precision(gains_rest, exponent_bits=8, mantissa_bits=7)
    gains_lo = gains_rest - gains_mid
    gains_parts = jnp.stack([gains_hi, gains_mid, gains_lo], axis=1).astype(jnp.bfloat16)
    gains_parts = gains_parts.reshape(per_chan, -1)
    row_both = gather_groups(jnp.concatenate([own_volt, gains_parts], axis=1), "col")
    row_count = n_cols * subant
    col_count = n_rows * subant
    row_left = row_both[:, :, :volt_size].reshape(per_chan, row_count, width)
    col_left = gather_groups(own_volt, "row").reshape(per_chan, col_count, width)
    row_swap = jnp.concatenate([row_left[:, :, samples:], -row_left[:, :, :samples]], axis=2)
    vis_re = (
        jnp.einsum("cqk,cpk->cqp", row_left, col_left, preferred_element_type=jnp.float32) / samples
    )
    vis_im = (
        jnp.einsum("cqk,cpk->cqp", row_swap, col_left, preferred_element_type=jnp.float32) / samples
    )
    row_pos = lax.dynamic_slice_in_dim(antenna_positions, row_index * n_cols, n_cols, 1).reshape(
        2, row_count
    )
    col_pos = lax.dynamic_index_in_dim(
        antenna_positions.reshape(2, n_rows, n_cols, subant), col_index, 2, keepdims=False
    ).reshape(2, col_count)
    row_flag = lax.dynamic_slice_in_dim(flagged, row_index * n_cols, n_cols, 0).reshape(row_count)
    own_flag = lax.dynamic_index_in_dim(flagged, row_index * n_cols + col_index, 0, keepdims=False)
    row_ids = row_index * n_cols * subant + jnp.arange(row_count, dtype=jnp.int32)
    col_ids = (
        (jnp.arange(n_rows, dtype=jnp.int32) * n_cols + col_index)[:, None] * subant
        + jnp.arange(subant, dtype=jnp.int32)[None, :]
    ).reshape(col_count)
    pixel_float = source_pixels.astype(jnp.float32)
    ell_coord = (pixel_float[:, 0] - 0.5 * PIX) / PIX
    emm_coord = (pixel_float[:, 1] - 0.5 * PIX) / PIX
    channel_ids = chan_index * per_chan + jnp.arange(per_chan, dtype=jnp.int32)
    frequencies = 1.0 + channel_ids.astype(jnp.float32) / (per_chan * n_chans)
    steer_re, steer_im = steering(row_pos, ell_coord, emm_coord, frequencies)
    far_re, far_im = steering(col_pos, ell_coord, emm_coord, frequencies)
    weight_re = (source_flux[:, None, :] * far_re).astype(jnp.bfloat16)
    weight_im = (source_flux[:, None, :] * far_im).astype(jnp.bfloat16)
    steer_both = jnp.concatenate([steer_re, steer_im], axis=2)
    steer_swap = jnp.concatenate([steer_im, -steer_re], axis=2)
    weight_both = jnp.concatenate([weight_re, weight_im], axis=2)
    model_re = jnp.einsum(
        "cqk,cpk->cqp", steer_both, weight_both, preferred_element_type=jnp.float32
    )
    model_im = jnp.einsum(
        "cqk,cpk->cqp", steer_swap, weight_both, preferred_element_type=jnp.float32
    )
    live = (1 - row_flag).astype(jnp.float32)
    apart = (row_ids[:, None] != col_ids[None, :]).astype(jnp.float32)
    keep = (live[:, None] * apart)[None, :, :]
    data_re = keep * (model_re * vis_re + model_im * vis_im)
    data_im = keep * (model_re * vis_im - model_im * vis_re)
    power = keep * (model_re * model_re + model_im * model_im)
    row_flags = row_flag.reshape(1, 1, n_cols, subant)
    parts = row_both[:, :, volt_size:].astype(jnp.float32).reshape(per_chan, n_cols, 3, 2, subant)
    row_gains = jnp.transpose((parts[:, :, 0] + parts[:, :, 1]) + parts[:, :, 2], (0, 2, 1, 3))
    for iteration in range(ITERS):
        gain_re = row_gains[:, 0].reshape(per_chan, row_count)
        gain_im = row_gains[:, 1].reshape(per_chan, row_count)
        weight_re = gain_re[:, :, None]
        weight_im = gain_im[:, :, None]
        num_re = jnp.sum(weight_re * data_re + weight_im * data_im, axis=1)
        num_im = jnp.sum(weight_re * data_im - weight_im * data_re, axis=1)
        denominator = jnp.sum((weight_re * weight_re + weight_im * weight_im) * power, axis=1)
        partial = jnp.stack([num_re, num_im, denominator], axis=0).reshape(3, per_chan, n_rows, subant)
        partial = jnp.transpose(partial, (2, 0, 1, 3))
        if iteration == ITERS - 1:
            incoming = lax.all_to_all(partial, "row", 0, 0, tiled=True)
            own_totals = incoming.sum(axis=0)
            fresh = jnp.stack(
                [
                    own_totals[0] / (own_totals[2] + small_eps),
                    -own_totals[1] / (own_totals[2] + small_eps),
                ],
                axis=1,
            )
            current = lax.dynamic_index_in_dim(row_gains, col_index, 2, keepdims=False)
            current = jnp.where(own_flag[None, None, :] == 1, current, 0.5 * (current + fresh))
            break
        outgoing = jnp.broadcast_to(
            partial[:, None], (n_rows, n_cols, 3, per_chan, subant)
        ).reshape(n_rows * n_cols, 3, per_chan, subant)
        incoming = lax.all_to_all(outgoing, ("row", "col"), 0, 0, tiled=True)
        totals = incoming.reshape(n_rows, n_cols, 3, per_chan, subant).sum(axis=0)
        total_re = jnp.transpose(totals[:, 0], (1, 0, 2))
        total_im = jnp.transpose(totals[:, 1], (1, 0, 2))
        total_den = jnp.transpose(totals[:, 2], (1, 0, 2))
        fresh = jnp.stack(
            [total_re / (total_den + small_eps), -total_im / (total_den + small_eps)], axis=1
        )
        row_gains = jnp.where(row_flags == 1, row_gains, 0.5 * (row_gains + fresh))
    return current[:, :, None, :]


def solution(mesh):
    in_specs = (
        P(("row", "col"), "chan", None, None, None),
        P("chan", None),
        P("chan", None, ("row", "col"), None),
        P(),
        P(),
        P(),
    )
    out_specs = P("chan", None, ("row", "col"), None)
    return jax.shard_map(
        on_device, mesh=mesh, in_specs=in_specs, out_specs=out_specs, check_vma=False
    )
```

```python
import math

import jax
import jax.numpy as jnp
from jax import lax
from jax.sharding import PartitionSpec as P

PIX = 256
ITERS = 3


phase_scale = 2.0 * math.pi * 8.0
small_eps = 1e-06


def steering(positions, ell_coord, emm_coord, frequencies):
    angle = (
        phase_scale
        * frequencies[:, None, None]
        * (
            positions[0][None, :, None] * ell_coord[None, None, :]
            + positions[1][None, :, None] * emm_coord[None, None, :]
        )
    )
    return (jnp.cos(angle).astype(jnp.bfloat16), (-jnp.sin(angle)).astype(jnp.bfloat16))


def gather_groups(block, axis):
    count = lax.axis_size(axis)
    outgoing = jnp.broadcast_to(block[:, None, :], (block.shape[0], count, block.shape[1]))
    return lax.all_to_all(outgoing, axis, 1, 1, tiled=True)


def on_device(voltages, source_flux, initial_gains, antenna_positions, flagged, source_pixels):
    n_rows = lax.axis_size("row")
    n_cols = lax.axis_size("col")
    n_chans = lax.axis_size("chan")
    row_index = lax.axis_index("row")
    col_index = lax.axis_index("col")
    chan_index = lax.axis_index("chan")
    subant = antenna_positions.shape[2]
    per_chan = source_flux.shape[0]
    samples = voltages.shape[3]
    count, own_ants, halves, _, all_chans = voltages.shape
    width = halves * samples
    local = jnp.transpose(voltages, (4, 0, 1, 2, 3)).reshape(all_chans, count * own_ants, width)
    own_volt = lax.all_to_all(local, "chan", split_axis=0, concat_axis=1, tiled=True)
    own_volt = own_volt.reshape(per_chan, subant * width)
    volt_size = subant * width
    gains_flat = initial_gains.reshape(per_chan, -1)
    gains_hi = lax.reduce_precision(gains_flat, exponent_bits=8, mantissa_bits=7)
    gains_rest = gains_flat - gains_hi
    gains_mid = lax.reduce_precision(gains_rest, exponent_bits=8, mantissa_bits=7)
    gains_lo = gains_rest - gains_mid
    gains_parts = jnp.stack([gains_hi, gains_mid, gains_lo], axis=1).astype(jnp.bfloat16)
    gains_parts = gains_parts.reshape(per_chan, -1)
    every = gather_groups(jnp.concatenate([own_volt, gains_parts], axis=1), ("row", "col"))
    row_both = lax.dynamic_slice_in_dim(every, row_index * n_cols, n_cols, 1)
    row_count = n_cols * subant
    col_count = n_rows * subant
    row_left = row_both[:, :, :volt_size].reshape(per_chan, row_count, width)
    col_both = lax.dynamic_index_in_dim(
        every.reshape(per_chan, n_rows, n_cols, every.shape[2]), col_index, 2, keepdims=False
    )
    col_left = col_both[:, :, :volt_size].reshape(per_chan, col_count, width)
    row_swap = jnp.concatenate([row_left[:, :, samples:], -row_left[:, :, :samples]], axis=2)
    vis_re = (
        jnp.einsum("cqk,cpk->cqp", row_left, col_left, preferred_element_type=jnp.float32) / samples
    )
    vis_im = (
        jnp.einsum("cqk,cpk->cqp", row_swap, col_left, preferred_element_type=jnp.float32) / samples
    )
    row_pos = lax.dynamic_slice_in_dim(antenna_positions, row_index * n_cols, n_cols, 1).reshape(
        2, row_count
    )
    col_pos = lax.dynamic_index_in_dim(
        antenna_positions.reshape(2, n_rows, n_cols, subant), col_index, 2, keepdims=False
    ).reshape(2, col_count)
    row_flag = lax.dynamic_slice_in_dim(flagged, row_index * n_cols, n_cols, 0).reshape(row_count)
    own_flag = lax.dynamic_index_in_dim(flagged, row_index * n_cols + col_index, 0, keepdims=False)
    row_ids = row_index * n_cols * subant + jnp.arange(row_count, dtype=jnp.int32)
    col_ids = (
        (jnp.arange(n_rows, dtype=jnp.int32) * n_cols + col_index)[:, None] * subant
        + jnp.arange(subant, dtype=jnp.int32)[None, :]
    ).reshape(col_count)
    pixel_float = source_pixels.astype(jnp.float32)
    ell_coord = (pixel_float[:, 0] - 0.5 * PIX) / PIX
    emm_coord = (pixel_float[:, 1] - 0.5 * PIX) / PIX
    channel_ids = chan_index * per_chan + jnp.arange(per_chan, dtype=jnp.int32)
    frequencies = 1.0 + channel_ids.astype(jnp.float32) / (per_chan * n_chans)
    steer_re, steer_im = steering(row_pos, ell_coord, emm_coord, frequencies)
    far_re, far_im = steering(col_pos, ell_coord, emm_coord, frequencies)
    weight_re = (source_flux[:, None, :] * far_re).astype(jnp.bfloat16)
    weight_im = (source_flux[:, None, :] * far_im).astype(jnp.bfloat16)
    steer_both = jnp.concatenate([steer_re, steer_im], axis=2)
    steer_swap = jnp.concatenate([steer_im, -steer_re], axis=2)
    weight_both = jnp.concatenate([weight_re, weight_im], axis=2)
    model_re = jnp.einsum(
        "cqk,cpk->cqp", steer_both, weight_both, preferred_element_type=jnp.float32
    )
    model_im = jnp.einsum(
        "cqk,cpk->cqp", steer_swap, weight_both, preferred_element_type=jnp.float32
    )
    live = (1 - row_flag).astype(jnp.float32)
    apart = (row_ids[:, None] != col_ids[None, :]).astype(jnp.float32)
    keep = (live[:, None] * apart)[None, :, :]
    data_re = keep * (model_re * vis_re + model_im * vis_im)
    data_im = keep * (model_re * vis_im - model_im * vis_re)
    power = keep * (model_re * model_re + model_im * model_im)
    row_flags = row_flag.reshape(1, 1, n_cols, subant)
    parts = row_both[:, :, volt_size:].astype(jnp.float32).reshape(per_chan, n_cols, 3, 2, subant)
    row_gains = jnp.transpose((parts[:, :, 0] + parts[:, :, 1]) + parts[:, :, 2], (0, 2, 1, 3))
    for iteration in range(ITERS):
        gain_re = row_gains[:, 0].reshape(per_chan, row_count)
        gain_im = row_gains[:, 1].reshape(per_chan, row_count)
        weight_re = gain_re[:, :, None]
        weight_im = gain_im[:, :, None]
        num_re = jnp.sum(weight_re * data_re + weight_im * data_im, axis=1)
        num_im = jnp.sum(weight_re * data_im - weight_im * data_re, axis=1)
        denominator = jnp.sum((weight_re * weight_re + weight_im * weight_im) * power, axis=1)
        partial = jnp.stack([num_re, num_im, denominator], axis=0).reshape(3, per_chan, n_rows, subant)
        partial = jnp.transpose(partial, (2, 0, 1, 3))
        if iteration == ITERS - 1:
            incoming = lax.all_to_all(partial, "row", 0, 0, tiled=True)
            own_totals = incoming.sum(axis=0)
            fresh = jnp.stack(
                [
                    own_totals[0] / (own_totals[2] + small_eps),
                    -own_totals[1] / (own_totals[2] + small_eps),
                ],
                axis=1,
            )
            current = lax.dynamic_index_in_dim(row_gains, col_index, 2, keepdims=False)
            current = jnp.where(own_flag[None, None, :] == 1, current, 0.5 * (current + fresh))
            break
        outgoing = jnp.broadcast_to(
            partial[:, None], (n_rows, n_cols, 3, per_chan, subant)
        ).reshape(n_rows * n_cols, 3, per_chan, subant)
        incoming = lax.all_to_all(outgoing, ("row", "col"), 0, 0, tiled=True)
        totals = incoming.reshape(n_rows, n_cols, 3, per_chan, subant).sum(axis=0)
        total_re = jnp.transpose(totals[:, 0], (1, 0, 2))
        total_im = jnp.transpose(totals[:, 1], (1, 0, 2))
        total_den = jnp.transpose(totals[:, 2], (1, 0, 2))
        fresh = jnp.stack(
            [total_re / (total_den + small_eps), -total_im / (total_den + small_eps)], axis=1
        )
        row_gains = jnp.where(row_flags == 1, row_gains, 0.5 * (row_gains + fresh))
    return current[:, :, None, :]


def solution(mesh):
    in_specs = (
        P(("row", "col"), "chan", None, None, None),
        P("chan", None),
        P("chan", None, ("row", "col"), None),
        P(),
        P(),
        P(),
    )
    out_specs = P("chan", None, ("row", "col"), None)
    return jax.shard_map(
        on_device, mesh=mesh, in_specs=in_specs, out_specs=out_specs, check_vma=False
    )
```

```python
import math

import jax
import jax.numpy as jnp
from jax import lax
from jax.sharding import PartitionSpec as P

PIX = 256
ITERS = 3


phase_scale = 2.0 * math.pi * 8.0
small_eps = 1e-06


def steering(positions, ell_coord, emm_coord, frequencies):
    angle = (
        phase_scale
        * frequencies[:, None, None]
        * (
            positions[0][None, :, None] * ell_coord[None, None, :]
            + positions[1][None, :, None] * emm_coord[None, None, :]
        )
    )
    return (jnp.cos(angle).astype(jnp.bfloat16), (-jnp.sin(angle)).astype(jnp.bfloat16))


def gather_groups(block, axis):
    count = lax.axis_size(axis)
    outgoing = jnp.broadcast_to(block[:, None, :], (block.shape[0], count, block.shape[1]))
    return lax.all_to_all(outgoing, axis, 1, 1, tiled=True)


def on_device(voltages, source_flux, initial_gains, antenna_positions, flagged, source_pixels):
    n_rows = lax.axis_size("row")
    n_cols = lax.axis_size("col")
    n_chans = lax.axis_size("chan")
    row_index = lax.axis_index("row")
    col_index = lax.axis_index("col")
    chan_index = lax.axis_index("chan")
    subant = antenna_positions.shape[2]
    per_chan = source_flux.shape[0]
    samples = voltages.shape[3]
    count, own_ants, halves, _, all_chans = voltages.shape
    width = halves * samples
    local = jnp.transpose(voltages, (4, 0, 1, 2, 3)).reshape(all_chans, count * own_ants, width)
    own_volt = lax.all_to_all(local, "chan", split_axis=0, concat_axis=1, tiled=True)
    own_volt = own_volt.reshape(per_chan, subant * width)
    volt_size = subant * width
    gains_flat = initial_gains.reshape(per_chan, -1)
    gains_hi = lax.reduce_precision(gains_flat, exponent_bits=8, mantissa_bits=7)
    gains_rest = gains_flat - gains_hi
    gains_mid = lax.reduce_precision(gains_rest, exponent_bits=8, mantissa_bits=7)
    gains_lo = gains_rest - gains_mid
    gains_parts = jnp.stack([gains_hi, gains_mid, gains_lo], axis=1).astype(jnp.bfloat16)
    gains_parts = gains_parts.reshape(per_chan, -1)
    row_both = gather_groups(jnp.concatenate([own_volt, gains_parts], axis=1), "col")
    row_count = n_cols * subant
    col_count = n_rows * subant
    row_left = row_both[:, :, :volt_size].reshape(per_chan, row_count, width)
    own_after = lax.optimization_barrier((row_both, own_volt))[1]
    col_left = gather_groups(own_after, "row").reshape(per_chan, col_count, width)
    row_swap = jnp.concatenate([row_left[:, :, samples:], -row_left[:, :, :samples]], axis=2)
    vis_re = (
        jnp.einsum("cqk,cpk->cqp", row_left, col_left, preferred_element_type=jnp.float32) / samples
    )
    vis_im = (
        jnp.einsum("cqk,cpk->cqp", row_swap, col_left, preferred_element_type=jnp.float32) / samples
    )
    row_pos = lax.dynamic_slice_in_dim(antenna_positions, row_index * n_cols, n_cols, 1).reshape(
        2, row_count
    )
    col_pos = lax.dynamic_index_in_dim(
        antenna_positions.reshape(2, n_rows, n_cols, subant), col_index, 2, keepdims=False
    ).reshape(2, col_count)
    row_flag = lax.dynamic_slice_in_dim(flagged, row_index * n_cols, n_cols, 0).reshape(row_count)
    own_flag = lax.dynamic_index_in_dim(flagged, row_index * n_cols + col_index, 0, keepdims=False)
    row_ids = row_index * n_cols * subant + jnp.arange(row_count, dtype=jnp.int32)
    col_ids = (
        (jnp.arange(n_rows, dtype=jnp.int32) * n_cols + col_index)[:, None] * subant
        + jnp.arange(subant, dtype=jnp.int32)[None, :]
    ).reshape(col_count)
    pixel_float = source_pixels.astype(jnp.float32)
    ell_coord = (pixel_float[:, 0] - 0.5 * PIX) / PIX
    emm_coord = (pixel_float[:, 1] - 0.5 * PIX) / PIX
    channel_ids = chan_index * per_chan + jnp.arange(per_chan, dtype=jnp.int32)
    frequencies = 1.0 + channel_ids.astype(jnp.float32) / (per_chan * n_chans)
    steer_re, steer_im = steering(row_pos, ell_coord, emm_coord, frequencies)
    far_re, far_im = steering(col_pos, ell_coord, emm_coord, frequencies)
    weight_re = (source_flux[:, None, :] * far_re).astype(jnp.bfloat16)
    weight_im = (source_flux[:, None, :] * far_im).astype(jnp.bfloat16)
    steer_both = jnp.concatenate([steer_re, steer_im], axis=2)
    steer_swap = jnp.concatenate([steer_im, -steer_re], axis=2)
    weight_both = jnp.concatenate([weight_re, weight_im], axis=2)
    model_re = jnp.einsum(
        "cqk,cpk->cqp", steer_both, weight_both, preferred_element_type=jnp.float32
    )
    model_im = jnp.einsum(
        "cqk,cpk->cqp", steer_swap, weight_both, preferred_element_type=jnp.float32
    )
    live = (1 - row_flag).astype(jnp.float32)
    apart = (row_ids[:, None] != col_ids[None, :]).astype(jnp.float32)
    keep = (live[:, None] * apart)[None, :, :]
    data_re = keep * (model_re * vis_re + model_im * vis_im)
    data_im = keep * (model_re * vis_im - model_im * vis_re)
    power = keep * (model_re * model_re + model_im * model_im)
    row_flags = row_flag.reshape(1, 1, n_cols, subant)
    parts = row_both[:, :, volt_size:].astype(jnp.float32).reshape(per_chan, n_cols, 3, 2, subant)
    row_gains = jnp.transpose((parts[:, :, 0] + parts[:, :, 1]) + parts[:, :, 2], (0, 2, 1, 3))
    for iteration in range(ITERS):
        gain_re = row_gains[:, 0].reshape(per_chan, row_count)
        gain_im = row_gains[:, 1].reshape(per_chan, row_count)
        weight_re = gain_re[:, :, None]
        weight_im = gain_im[:, :, None]
        num_re = jnp.sum(weight_re * data_re + weight_im * data_im, axis=1)
        num_im = jnp.sum(weight_re * data_im - weight_im * data_re, axis=1)
        denominator = jnp.sum((weight_re * weight_re + weight_im * weight_im) * power, axis=1)
        partial = jnp.stack([num_re, num_im, denominator], axis=0).reshape(3, per_chan, n_rows, subant)
        partial = jnp.transpose(partial, (2, 0, 1, 3))
        if iteration == ITERS - 1:
            incoming = lax.all_to_all(partial, "row", 0, 0, tiled=True)
            own_totals = incoming.sum(axis=0)
            fresh = jnp.stack(
                [
                    own_totals[0] / (own_totals[2] + small_eps),
                    -own_totals[1] / (own_totals[2] + small_eps),
                ],
                axis=1,
            )
            current = lax.dynamic_index_in_dim(row_gains, col_index, 2, keepdims=False)
            current = jnp.where(own_flag[None, None, :] == 1, current, 0.5 * (current + fresh))
            break
        outgoing = jnp.broadcast_to(
            partial[:, None], (n_rows, n_cols, 3, per_chan, subant)
        ).reshape(n_rows * n_cols, 3, per_chan, subant)
        incoming = lax.all_to_all(outgoing, ("row", "col"), 0, 0, tiled=True)
        totals = incoming.reshape(n_rows, n_cols, 3, per_chan, subant).sum(axis=0)
        total_re = jnp.transpose(totals[:, 0], (1, 0, 2))
        total_im = jnp.transpose(totals[:, 1], (1, 0, 2))
        total_den = jnp.transpose(totals[:, 2], (1, 0, 2))
        fresh = jnp.stack(
            [total_re / (total_den + small_eps), -total_im / (total_den + small_eps)], axis=1
        )
        row_gains = jnp.where(row_flags == 1, row_gains, 0.5 * (row_gains + fresh))
    return current[:, :, None, :]


def solution(mesh):
    in_specs = (
        P(("row", "col"), "chan", None, None, None),
        P("chan", None),
        P("chan", None, ("row", "col"), None),
        P(),
        P(),
        P(),
    )
    out_specs = P("chan", None, ("row", "col"), None)
    return jax.shard_map(
        on_device, mesh=mesh, in_specs=in_specs, out_specs=out_specs, check_vma=False
    )
```
